32 devices in a mesh: blk: 8 (over z, y), grp: 4 (over x, core).
Axes of the slice: x: 2, y: 2, z: 4, core: 2. Of those that a mesh axis runs over, the one named last changes fastest.
Arguments:
- state: float32 [2, 128, 4096], P(None, None, ('blk', 'grp')), may hold values from -3 to 3
- prev_slope: float32 [2, 128, 4096], P(None, None, ('blk', 'grp')), may hold values from -4 to 4
- positions: float32 [2, 4096], P(None, ('blk', 'grp')), may hold values from -1 to 1
- pump: float32 [4096], P(('blk', 'grp')), may hold values from -0.5 to 1.5
- detuning: float32 [4096], P(('blk', 'grp')), may hold values from -4 to 4
- kappa: float32 [6, 4096], P(None, ('blk', 'grp')), may hold values from 0.2 to 1
- neighbours: int32 [6, 4096], P(None, ('blk', 'grp')), may hold values from 0 to 255
- send_list: int32 [2, 2048], P(None, ('blk', 'grp')), may hold values from 0 to 127
Outputs:
- slope: float32 [2, 128, 4096], P(None, None, ('blk', 'grp'))
The draws below stay inside these ranges and needn't reach their ends.
Inputs may be any that keep to these rules, and one draw needn't show every extreme that they name: `neighbours`: places below 128 are the block's own emitters, the next 64 those listed by the previous block, the last 64 those listed by the next block. `send_list`: places in the listing block.
All inputs are finite; a program needn't handle non-finite values.
Results may differ from the reference program's by a relative error of at most 0.0012.
Values may be sent and summed in bfloat16 or wider, within the bound.
No kernel may reach another device: no remote copies, remote signals or barrier semaphores. Data moves between devices by JAX's collectives and lax.ppermute only.
A program may use at most 64 MiB of HBM per device.

```python
import math
import jax
import jax.numpy as jnp
from jax import lax

ROWS = 128
MEMBERS = 128
NEIGH = 6
HALO = 64
EMITTERS = 4096
DEVICES = 32


def with_ends(result, key, least, high):
    spot = [jax.random.randint(jax.random.fold_in(key, axis), (), 0, length) for axis, length in enumerate(result.shape)]
    widest = result.shape.index(max(result.shape))
    neighbour = spot[:widest] + [(spot[widest] + 1) % result.shape[widest]] + spot[widest + 1:]
    return result.at[tuple(spot)].set(least).at[tuple(neighbour)].set(high)


def level_of(key, extent, shards, low, largest):
    def one(dim, blocks):
        heights = jax.random.uniform(jax.random.fold_in(jax.random.fold_in(key, 6), dim), (blocks,), jnp.float32, low / len(shards), largest / len(shards))
        return jnp.repeat(jnp.exp(heights), extent[dim] // blocks).reshape((-1,) + (1,) * (len(extent) - dim - 1))

    loudness = one(*shards[0])
    for cut in shards[1:]:
        loudness = loudness * one(*cut)
    return loudness


def scatter_about(rng, shape, width, limit, pieces=(), kind=jnp.bfloat16):
    loudness = level_of(rng, shape, pieces, -0.22, 0.18) if pieces else 1.0
    drawn = jax.random.normal(rng, shape, jnp.float32) * width * loudness
    return jnp.minimum(jnp.maximum(drawn, -limit), limit).astype(kind)


def setup_inputs(seed: int = 0) -> dict:
    arg_keys = jax.random.split(jax.random.key(seed), 9)
    state = scatter_about(arg_keys[0], (2, MEMBERS, EMITTERS), 0.5, 3.0, ((2, 32),), jnp.float32)
    prev_slope = scatter_about(arg_keys[1], (2, MEMBERS, EMITTERS), 0.6, 4.0, ((2, 32),), jnp.float32)
    positions = jnp.clip(jax.random.uniform(arg_keys[2], (2, EMITTERS), jnp.float32, -1.0, 1.0) * level_of(arg_keys[2], (2, EMITTERS), ((1, 32),), -0.4, 0.0), -1.0, 1.0)
    pump = jnp.clip(-0.5 + 2.0 * jax.random.uniform(arg_keys[3], (EMITTERS,), jnp.float32) ** level_of(arg_keys[3], (EMITTERS,), ((0, 32),), -0.2, 0.2), -0.5, 1.5)
    detuning = scatter_about(arg_keys[4], (EMITTERS,), 1.0, 4.0, ((0, 32),), jnp.float32)
    kappa = jnp.clip(jnp.exp(math.log(1.0) - 1.609438 * jax.random.uniform(arg_keys[5], (NEIGH, EMITTERS), jnp.float32) ** level_of(arg_keys[5], (NEIGH, EMITTERS), ((1, 32),), -0.2, 0.2)), 0.2, 1.0)
    neighbours = with_ends(jax.random.randint(arg_keys[6], (NEIGH, EMITTERS), 0, ROWS + 2 * HALO), jax.random.fold_in(arg_keys[6], 1), 0, (ROWS + 2 * HALO) - 1).astype(jnp.int32)
    send_list = with_ends(jax.random.randint(arg_keys[7], (2, HALO * DEVICES), 0, ROWS), jax.random.fold_in(arg_keys[7], 1), 0, ROWS - 1).astype(jnp.int32)
    return dict(state=state, prev_slope=prev_slope, positions=positions, pump=pump, detuning=detuning, kappa=kappa, neighbours=neighbours, send_list=send_list)


section_weight = 0.25
phase_rate = 60.0
alpha_factor = 2.0

def kernel_table(source_place, target_place, scaled):
    horizontal = target_place[0][None, :] - source_place[0][:, None]
    vertical = target_place[1][None, :] - source_place[1][:, None]
    phase = phase_rate * (horizontal * horizontal + vertical * vertical)
    cosine = (scaled * jnp.cos(phase)).astype(jnp.bfloat16)
    sine_part = (scaled * jnp.sin(phase)).astype(jnp.bfloat16)
    return jnp.concatenate([cosine, sine_part], axis=1)

def block_columns(total, fields, source_place, target_place, scaled):
    members = fields.shape[1]
    targets = target_place.shape[1]
    kernel = kernel_table(source_place, target_place, scaled)
    flat = fields.reshape(2 * members, fields.shape[2])
    product = jnp.dot(flat, kernel, preferred_element_type=jnp.float32)
    real_part = product[:members, :targets] - product[members:, targets:]
    imag_part = product[:members, targets:] + product[members:, :targets]
    return total + jnp.stack([real_part, imag_part])

def reference(state, prev_slope, positions, pump, detuning, kappa, neighbours, send_list):
    section_field = state + section_weight * prev_slope
    section_half = section_field.astype(jnp.bfloat16)
    scaled = 1.0 / math.sqrt(EMITTERS)

    def one_block(block_index, total):
        fields = lax.dynamic_slice_in_dim(section_half, block_index * ROWS, ROWS, 2)
        source_place = lax.dynamic_slice_in_dim(positions, block_index * ROWS, ROWS, 1)
        return block_columns(total, fields, source_place, positions, scaled)
    empty = jnp.zeros((2, MEMBERS, EMITTERS), jnp.float32)
    fresnel = lax.fori_loop(0, DEVICES, one_block, empty)
    blocked = section_field.reshape(2, MEMBERS, DEVICES, ROWS)
    lists = send_list.reshape(2, DEVICES, HALO)
    next_index = jnp.broadcast_to(lists[0][None, None], (2, MEMBERS, DEVICES, HALO))
    prev_index = jnp.broadcast_to(lists[1][None, None], (2, MEMBERS, DEVICES, HALO))
    to_next = jnp.take_along_axis(blocked, next_index, axis=3)
    to_prev = jnp.take_along_axis(blocked, prev_index, axis=3)
    zero_block = jnp.zeros((2, MEMBERS, 1, HALO), jnp.float32)
    from_prev = jnp.concatenate([zero_block, to_next[:, :, :-1]], axis=2)
    from_next = jnp.concatenate([to_prev[:, :, 1:], zero_block], axis=2)
    whole_buffer = jnp.concatenate([blocked, from_prev, from_next], axis=3)
    neighbour_blocks = neighbours.reshape(NEIGH, DEVICES, ROWS)
    coupled = jnp.zeros((2, MEMBERS, EMITTERS), jnp.float32)
    for neighbour_slot in range(NEIGH):
        index_full = jnp.broadcast_to(neighbour_blocks[neighbour_slot][None, None], (2, MEMBERS, DEVICES, ROWS))
        picked = jnp.take_along_axis(whole_buffer, index_full, axis=3).reshape(2, MEMBERS, EMITTERS)
        coupled = coupled + kappa[neighbour_slot] * picked
    real_field = section_field[0]
    imag_field = section_field[1]
    modulus = real_field * real_field + imag_field * imag_field
    linear_real = pump - modulus
    linear_imag = detuning - alpha_factor * modulus
    local_real = linear_real * real_field - linear_imag * imag_field
    local_imag = linear_real * imag_field + linear_imag * real_field
    slope_real = local_real + fresnel[0] - coupled[1]
    slope_imag = local_imag + fresnel[1] + coupled[0]
    return jnp.stack([slope_real, slope_imag])
```

```python
import math

import jax
import jax.numpy as jnp
from jax import lax
from jax.sharding import PartitionSpec as P

section_weight = 0.25
phase_rate = 60.0
alpha_factor = 2.0
ALL = ("blk", "grp")


def bf16_pieces(value):
    high = lax.reduce_precision(value, exponent_bits=8, mantissa_bits=7)
    rest = value - high
    middle = lax.reduce_precision(rest, exponent_bits=8, mantissa_bits=7)
    low = rest - middle
    return [p.astype(jnp.bfloat16) for p in (high, middle, low)]


def from_pieces(high, middle, low):
    f32 = jnp.float32
    return high.astype(f32) + (middle.astype(f32) + low.astype(f32))


def kernel_table(source_place, target_place, scaled):
    horizontal = target_place[0][None, :] - source_place[0][:, None]
    vertical = target_place[1][None, :] - source_place[1][:, None]
    phase = phase_rate * (horizontal * horizontal + vertical * vertical)
    cosine = (scaled * jnp.cos(phase)).astype(jnp.bfloat16)
    sine_part = (scaled * jnp.sin(phase)).astype(jnp.bfloat16)
    return jnp.concatenate([cosine, sine_part], axis=1)


def block_product(fields, source_place, target_place, scaled):
    kernel = kernel_table(source_place, target_place, scaled)
    flat = fields.reshape(2 * fields.shape[1], fields.shape[2])
    return jnp.dot(flat, kernel, preferred_element_type=jnp.float32)


def local(state, prev_slope, positions, pump, detuning, kappa, neighbours, send_list):
    members = state.shape[1]
    rows_here = state.shape[2]
    devices = lax.axis_size(ALL)
    scaled = 1.0 / math.sqrt(rows_here * devices)
    section_field = state + section_weight * prev_slope
    section_half = section_field.astype(jnp.bfloat16)

    to_prev = jnp.take(section_field, send_list[1], axis=2)
    to_next = jnp.take(section_field, send_list[0], axis=2)
    from_prev = lax.ppermute(to_next, ALL, [(i, i + 1) for i in range(devices - 1)])
    from_next = lax.ppermute(to_prev, ALL, [(i + 1, i) for i in range(devices - 1)])

    pieces = jnp.stack(bf16_pieces(positions), axis=1)
    payload = jnp.concatenate([section_half, pieces], axis=1)

    product = block_product(section_half, positions, positions, scaled)
    gathered = payload
    mask = devices // 2
    while mask >= 1:
        received = lax.ppermute(gathered, ALL, [(i, i ^ mask) for i in range(devices)])
        place = from_pieces(
            received[:, members], received[:, members + 1], received[:, members + 2]
        )
        product = product + block_product(received[:, :members], place, positions, scaled)
        gathered = jnp.concatenate([gathered, received], axis=2)
        mask //= 2
    real_part = product[:members, :rows_here] - product[members:, rows_here:]
    imag_part = product[:members, rows_here:] + product[members:, :rows_here]

    local_buffer = jnp.concatenate([section_field, from_prev, from_next], axis=2)
    coupled = jnp.zeros((2, members, rows_here), jnp.float32)
    for neighbour_slot in range(kappa.shape[0]):
        picked = jnp.take(local_buffer, neighbours[neighbour_slot], axis=2)
        coupled = coupled + kappa[neighbour_slot] * picked
    real_field = section_field[0]
    imag_field = section_field[1]
    modulus = real_field * real_field + imag_field * imag_field
    linear_real = pump - modulus
    linear_imag = detuning - alpha_factor * modulus
    local_real = linear_real * real_field - linear_imag * imag_field
    local_imag = linear_real * imag_field + linear_imag * real_field
    slope_real = local_real + real_part - coupled[1]
    slope_imag = local_imag + imag_part + coupled[0]
    return jnp.stack([slope_real, slope_imag])


def solution(mesh):
    placed = (
        P(None, None, ALL),
        P(None, None, ALL),
        P(None, ALL),
        P(ALL),
        P(ALL),
        P(None, ALL),
        P(None, ALL),
        P(None, ALL),
    )
    return jax.shard_map(
        local, mesh=mesh, in_specs=placed, out_specs=P(None, None, ALL), check_vma=False
    )
```

```python
import math

import jax
import jax.numpy as jnp
from jax import lax
from jax.sharding import PartitionSpec as P

section_weight = 0.25
phase_rate = 60.0
alpha_factor = 2.0
ALL = ("blk", "grp")


def bf16_pieces(value):
    high = lax.reduce_precision(value, exponent_bits=8, mantissa_bits=7)
    rest = value - high
    middle = lax.reduce_precision(rest, exponent_bits=8, mantissa_bits=7)
    low = rest - middle
    return [p.astype(jnp.bfloat16) for p in (high, middle, low)]


def from_pieces(high, middle, low):
    f32 = jnp.float32
    return high.astype(f32) + (middle.astype(f32) + low.astype(f32))


def kernel_table(source_place, target_place, scaled):
    horizontal = target_place[0][None, :] - source_place[0][:, None]
    vertical = target_place[1][None, :] - source_place[1][:, None]
    phase = phase_rate * (horizontal * horizontal + vertical * vertical)
    cosine = (scaled * jnp.cos(phase)).astype(jnp.bfloat16)
    sine_part = (scaled * jnp.sin(phase)).astype(jnp.bfloat16)
    return jnp.concatenate([cosine, sine_part], axis=1)


def block_product(fields, source_place, target_place, scaled):
    kernel = kernel_table(source_place, target_place, scaled)
    flat = fields.reshape(2 * fields.shape[1], fields.shape[2])
    return jnp.dot(flat, kernel, preferred_element_type=jnp.float32)


def exchange(value, axis, mask):
    count = lax.axis_size(axis)
    return lax.ppermute(value, axis, [(i, i ^ mask) for i in range(count)])


def local(state, prev_slope, positions, pump, detuning, kappa, neighbours, send_list):
    members = state.shape[1]
    rows_here = state.shape[2]
    devices = lax.axis_size(ALL)
    blocks = lax.axis_size("blk")
    group = lax.axis_size("grp")
    scaled = 1.0 / math.sqrt(rows_here * devices)
    section_field = state + section_weight * prev_slope
    section_half = section_field.astype(jnp.bfloat16)
    where_in_group = lax.axis_index("grp")

    to_prev = jnp.take(section_field, send_list[1], axis=2)
    to_next = jnp.take(section_field, send_list[0], axis=2)
    from_prev = lax.ppermute(to_next, ALL, [(i, i + 1) for i in range(devices - 1)])
    from_next = lax.ppermute(to_prev, ALL, [(i + 1, i) for i in range(devices - 1)])

    targets = positions
    mask = 1
    while mask < group:
        other = exchange(targets, "grp", mask)
        upper = (where_in_group & mask) != 0
        targets = jnp.where(
            upper,
            jnp.concatenate([other, targets], axis=1),
            jnp.concatenate([targets, other], axis=1),
        )
        mask *= 2
    width = targets.shape[1]

    pieces = jnp.stack(bf16_pieces(positions), axis=1)
    payload = jnp.concatenate([section_half, pieces], axis=1)
    product = block_product(section_half, positions, targets, scaled)
    gathered = payload
    mask = blocks // 2
    while mask >= 1:
        received = exchange(gathered, "blk", mask)
        place = from_pieces(
            received[:, members], received[:, members + 1], received[:, members + 2]
        )
        product = product + block_product(received[:, :members], place, targets, scaled)
        gathered = jnp.concatenate([gathered, received], axis=2)
        mask //= 2
    partial = jnp.stack(
        [
            product[:members, :width] - product[members:, width:],
            product[:members, width:] + product[members:, :width],
        ]
    )

    mask = group // 2
    while mask >= 1:
        half = partial.shape[2] // 2
        lower = partial[:, :, :half]
        higher = partial[:, :, half:]
        upper = (where_in_group & mask) != 0
        keep = jnp.where(upper, higher, lower)
        give = jnp.where(upper, lower, higher)
        partial = keep + exchange(give, "grp", mask)
        mask //= 2
    real_part = partial[0]
    imag_part = partial[1]

    local_buffer = jnp.concatenate([section_field, from_prev, from_next], axis=2)
    coupled = jnp.zeros((2, members, rows_here), jnp.float32)
    for neighbour_slot in range(kappa.shape[0]):
        picked = jnp.take(local_buffer, neighbours[neighbour_slot], axis=2)
        coupled = coupled + kappa[neighbour_slot] * picked
    real_field = section_field[0]
    imag_field = section_field[1]
    modulus = real_field * real_field + imag_field * imag_field
    linear_real = pump - modulus
    linear_imag = detuning - alpha_factor * modulus
    local_real = linear_real * real_field - linear_imag * imag_field
    local_imag = linear_real * imag_field + linear_imag * real_field
    slope_real = local_real + real_part - coupled[1]
    slope_imag = local_imag + imag_part + coupled[0]
    return jnp.stack([slope_real, slope_imag])


def solution(mesh):
    placed = (
        P(None, None, ALL),
        P(None, None, ALL),
        P(None, ALL),
        P(ALL),
        P(ALL),
        P(None, ALL),
        P(None, ALL),
        P(None, ALL),
    )
    return jax.shard_map(
        local, mesh=mesh, in_specs=placed, out_specs=P(None, None, ALL), check_vma=False
    )
```

```python
import math

import jax
import jax.numpy as jnp
from jax import lax
from jax.sharding import PartitionSpec as P

section_weight = 0.25
phase_rate = 60.0
alpha_factor = 2.0
ALL = ("blk", "grp")


def bf16_pieces(value):
    high = lax.reduce_precision(value, exponent_bits=8, mantissa_bits=7)
    rest = value - high
    middle = lax.reduce_precision(rest, exponent_bits=8, mantissa_bits=7)
    low = rest - middle
    return [p.astype(jnp.bfloat16) for p in (high, middle, low)]


def from_pieces(high, middle, low):
    f32 = jnp.float32
    return high.astype(f32) + (middle.astype(f32) + low.astype(f32))


def kernel_table(source_place, target_place, scaled):
    horizontal = target_place[0][None, :] - source_place[0][:, None]
    vertical = target_place[1][None, :] - source_place[1][:, None]
    phase = phase_rate * (horizontal * horizontal + vertical * vertical)
    cosine = (scaled * jnp.cos(phase)).astype(jnp.bfloat16)
    sine_part = (scaled * jnp.sin(phase)).astype(jnp.bfloat16)
    return jnp.concatenate([cosine, sine_part], axis=1)


def block_product(fields, source_place, target_place, scaled):
    kernel = kernel_table(source_place, target_place, scaled)
    flat = fields.reshape(2 * fields.shape[1], fields.shape[2])
    return jnp.dot(flat, kernel, preferred_element_type=jnp.float32)


def exchange(value, axis, mask):
    count = lax.axis_size(axis)
    return lax.ppermute(value, axis, [(i, i ^ mask) for i in range(count)])


def local(state, prev_slope, positions, pump, detuning, kappa, neighbours, send_list):
    members = state.shape[1]
    rows_here = state.shape[2]
    devices = lax.axis_size(ALL)
    blocks = lax.axis_size("blk")
    group = lax.axis_size("grp")
    scaled = 1.0 / math.sqrt(rows_here * devices)
    section_field = state + section_weight * prev_slope
    section_half = section_field.astype(jnp.bfloat16)
    where_in_group = lax.axis_index("grp")

    me = lax.axis_index(ALL)
    odd = (me % 2) == 1
    lists = jnp.take(section_field, jnp.concatenate([send_list[1], send_list[0]]), axis=2)
    halo_width = send_list.shape[1]
    to_prev = lists[:, :, :halo_width]
    to_next = lists[:, :, halo_width:]
    paired = jnp.where(odd, to_prev, to_next)
    crossed = jnp.where(odd, to_next, to_prev)
    crossing = [(i, i + 1) for i in range(1, devices - 1, 2)]
    crossing += [(i, i - 1) for i in range(2, devices, 2)]
    from_crossed = lax.ppermute(crossed, ALL, crossing)

    coded = positions.reshape(2, rows_here // halo_width, halo_width)
    first = exchange(jnp.concatenate([paired, coded], axis=1), "grp", 1)
    from_paired = first[:, :members]
    other = first[:, members:].reshape(2, rows_here)
    targets = jnp.where(
        odd,
        jnp.concatenate([other, positions], axis=1),
        jnp.concatenate([positions, other], axis=1),
    )
    mask = 2
    while mask < group:
        other = exchange(targets, "grp", mask)
        upper = (where_in_group & mask) != 0
        targets = jnp.where(
            upper,
            jnp.concatenate([other, targets], axis=1),
            jnp.concatenate([targets, other], axis=1),
        )
        mask *= 2
    width = targets.shape[1]
    from_prev = jnp.where(odd, from_paired, from_crossed)
    from_next = jnp.where(odd, from_crossed, from_paired)

    pieces = jnp.stack(bf16_pieces(positions), axis=1)
    payload = jnp.concatenate([section_half, pieces], axis=1)
    product = block_product(section_half, positions, targets, scaled)
    gathered = payload
    mask = blocks // 2
    while mask >= 1:
        received = exchange(gathered, "blk", mask)
        place = from_pieces(
            received[:, members], received[:, members + 1], received[:, members + 2]
        )
        product = product + block_product(received[:, :members], place, targets, scaled)
        gathered = jnp.concatenate([gathered, received], axis=2)
        mask //= 2
    partial = jnp.stack(
        [
            product[:members, :width] - product[members:, width:],
            product[:members, width:] + product[members:, :width],
        ]
    )

    mask = group // 2
    while mask >= 1:
        half = partial.shape[2] // 2
        lower = partial[:, :, :half]
        higher = partial[:, :, half:]
        upper = (where_in_group & mask) != 0
        keep = jnp.where(upper, higher, lower)
        give = jnp.where(upper, lower, higher)
        partial = keep + exchange(give, "grp", mask)
        mask //= 2
    real_part = partial[0]
    imag_part = partial[1]

    local_buffer = jnp.concatenate([section_field, from_prev, from_next], axis=2)
    places = local_buffer.shape[2]
    hit = neighbours[:, None, :] == lax.broadcasted_iota(jnp.int32, (1, places, 1), 1)
    weights = jnp.sum(jnp.where(hit, kappa[:, None, :], 0.0), axis=0)
    coupled = jnp.dot(
        local_buffer.reshape(2 * members, places),
        weights,
        precision=lax.Precision.HIGHEST,
        preferred_element_type=jnp.float32,
    ).reshape(2, members, rows_here)
    real_field = section_field[0]
    imag_field = section_field[1]
    modulus = real_field * real_field + imag_field * imag_field
    linear_real = pump - modulus
    linear_imag = detuning - alpha_factor * modulus
    local_real = linear_real * real_field - linear_imag * imag_field
    local_imag = linear_real * imag_field + linear_imag * real_field
    slope_real = local_real + real_part - coupled[1]
    slope_imag = local_imag + imag_part + coupled[0]
    return jnp.stack([slope_real, slope_imag])


def solution(mesh):
    placed = (
        P(None, None, ALL),
        P(None, None, ALL),
        P(None, ALL),
        P(ALL),
        P(ALL),
        P(None, ALL),
        P(None, ALL),
        P(None, ALL),
    )
    return jax.shard_map(
        local, mesh=mesh, in_specs=placed, out_specs=P(None, None, ALL), check_vma=False
    )
```

```python
import math

import jax
import jax.numpy as jnp
from jax import lax
from jax.sharding import PartitionSpec as P

section_weight = 0.25
phase_rate = 60.0
alpha_factor = 2.0
ALL = ("blk", "grp")


def bf16_pieces(value):
    high = lax.reduce_precision(value, exponent_bits=8, mantissa_bits=7)
    rest = value - high
    middle = lax.reduce_precision(rest, exponent_bits=8, mantissa_bits=7)
    low = rest - middle
    return [p.astype(jnp.bfloat16) for p in (high, middle, low)]


def from_pieces(high, middle, low):
    f32 = jnp.float32
    return high.astype(f32) + (middle.astype(f32) + low.astype(f32))


def kernel_table(source_place, target_place, scaled):
    horizontal = target_place[0][None, :] - source_place[0][:, None]
    vertical = target_place[1][None, :] - source_place[1][:, None]
    phase = phase_rate * (horizontal * horizontal + vertical * vertical)
    cosine = (scaled * jnp.cos(phase)).astype(jnp.bfloat16)
    sine_part = (scaled * jnp.sin(phase)).astype(jnp.bfloat16)
    return jnp.concatenate([cosine, sine_part], axis=1)


def block_product(fields, source_place, target_place, scaled):
    kernel = kernel_table(source_place, target_place, scaled)
    flat = fields.reshape(2 * fields.shape[1], fields.shape[2])
    return jnp.dot(flat, kernel, preferred_element_type=jnp.float32)


def exchange(value, axis, mask):
    count = lax.axis_size(axis)
    return lax.ppermute(value, axis, [(i, i ^ mask) for i in range(count)])


def local(state, prev_slope, positions, pump, detuning, kappa, neighbours, send_list):
    members = state.shape[1]
    rows_here = state.shape[2]
    devices = lax.axis_size(ALL)
    blocks = lax.axis_size("blk")
    group = lax.axis_size("grp")
    scaled = 1.0 / math.sqrt(rows_here * devices)
    section_field = state + section_weight * prev_slope
    section_half = section_field.astype(jnp.bfloat16)
    where_in_group = lax.axis_index("grp")

    me = lax.axis_index(ALL)
    odd = (me % 2) == 1
    listed = jnp.concatenate([send_list[1], send_list[0]])
    pick = (lax.broadcasted_iota(jnp.int32, (rows_here, 1), 0) == listed[None, :]).astype(jnp.float32)
    lists = jnp.dot(
        section_field.reshape(2 * members, rows_here),
        pick,
        precision=lax.Precision.HIGHEST,
        preferred_element_type=jnp.float32,
    ).reshape(2, members, -1)
    halo_width = send_list.shape[1]
    to_prev = lists[:, :, :halo_width]
    to_next = lists[:, :, halo_width:]
    paired = jnp.where(odd, to_prev, to_next)
    crossed = jnp.where(odd, to_next, to_prev)
    crossing = [(i, i + 1) for i in range(1, devices - 1, 2)]
    crossing += [(i, i - 1) for i in range(2, devices, 2)]
    from_crossed = lax.ppermute(crossed, ALL, crossing)

    coded = positions.reshape(2, rows_here // halo_width, halo_width)
    first = exchange(jnp.concatenate([paired, coded], axis=1), "grp", 1)
    from_paired = first[:, :members]
    other = first[:, members:].reshape(2, rows_here)
    targets = jnp.where(
        odd,
        jnp.concatenate([other, positions], axis=1),
        jnp.concatenate([positions, other], axis=1),
    )
    mask = 2
    while mask < group:
        other = exchange(targets, "grp", mask)
        upper = (where_in_group & mask) != 0
        targets = jnp.where(
            upper,
            jnp.concatenate([other, targets], axis=1),
            jnp.concatenate([targets, other], axis=1),
        )
        mask *= 2
    width = targets.shape[1]
    from_prev = jnp.where(odd, from_paired, from_crossed)
    from_next = jnp.where(odd, from_crossed, from_paired)

    pieces = jnp.stack(bf16_pieces(positions), axis=1)
    payload = jnp.concatenate([section_half, pieces], axis=1)
    product = block_product(section_half, positions, targets, scaled)
    gathered = payload
    mask = blocks // 2
    while mask >= 1:
        received = exchange(gathered, "blk", mask)
        place = from_pieces(
            received[:, members], received[:, members + 1], received[:, members + 2]
        )
        product = product + block_product(received[:, :members], place, targets, scaled)
        gathered = jnp.concatenate([gathered, received], axis=2)
        mask //= 2
    partial = jnp.stack(
        [
            product[:members, :width] - product[members:, width:],
            product[:members, width:] + product[members:, :width],
        ]
    )

    count = group
    mask = 1
    while mask < group:
        split = partial.reshape(2, members, count // 2, 2, rows_here)
        upper = (where_in_group & mask) != 0
        keep = jnp.where(upper, split[:, :, :, 1], split[:, :, :, 0])
        give = jnp.where(upper, split[:, :, :, 0], split[:, :, :, 1])
        partial = (keep + exchange(give, "grp", mask)).reshape(2, members, -1)
        count //= 2
        mask *= 2
    real_part = partial[0]
    imag_part = partial[1]

    local_buffer = jnp.concatenate([section_field, from_prev, from_next], axis=2)
    places = local_buffer.shape[2]
    hit = neighbours[:, None, :] == lax.broadcasted_iota(jnp.int32, (1, places, 1), 1)
    weights = jnp.sum(jnp.where(hit, kappa[:, None, :], 0.0), axis=0)
    coupled = jnp.dot(
        local_buffer.reshape(2 * members, places),
        weights,
        precision=lax.Precision.HIGHEST,
        preferred_element_type=jnp.float32,
    ).reshape(2, members, rows_here)
    real_field = section_field[0]
    imag_field = section_field[1]
    modulus = real_field * real_field + imag_field * imag_field
    linear_real = pump - modulus
    linear_imag = detuning - alpha_factor * modulus
    local_real = linear_real * real_field - linear_imag * imag_field
    local_imag = linear_real * imag_field + linear_imag * real_field
    slope_real = local_real + real_part - coupled[1]
    slope_imag = local_imag + imag_part + coupled[0]
    return jnp.stack([slope_real, slope_imag])


def solution(mesh):
    placed = (
        P(None, None, ALL),
        P(None, None, ALL),
        P(None, ALL),
        P(ALL),
        P(ALL),
        P(None, ALL),
        P(None, ALL),
        P(None, ALL),
    )
    return jax.shard_map(
        local, mesh=mesh, in_specs=placed, out_specs=P(None, None, ALL), check_vma=False
    )
```

```python
import math

import jax
import jax.numpy as jnp
from jax import lax
from jax.sharding import PartitionSpec as P

section_weight = 0.25
phase_rate = 60.0
alpha_factor = 2.0
ALL = ("blk", "grp")


def bf16_pieces(value):
    high = lax.reduce_precision(value, exponent_bits=8, mantissa_bits=7)
    rest = value - high
    middle = lax.reduce_precision(rest, exponent_bits=8, mantissa_bits=7)
    low = rest - middle
    return [p.astype(jnp.bfloat16) for p in (high, middle, low)]


def from_pieces(high, middle, low):
    f32 = jnp.float32
    return high.astype(f32) + (middle.astype(f32) + low.astype(f32))


def kernel_table(source_place, target_place, scaled):
    horizontal = target_place[0][None, :] - source_place[0][:, None]
    vertical = target_place[1][None, :] - source_place[1][:, None]
    phase = phase_rate * (horizontal * horizontal + vertical * vertical)
    cosine = (scaled * jnp.cos(phase)).astype(jnp.bfloat16)
    sine_part = (scaled * jnp.sin(phase)).astype(jnp.bfloat16)
    return jnp.concatenate([cosine, sine_part], axis=1)


def block_product(fields, source_place, target_place, scaled):
    kernel = kernel_table(source_place, target_place, scaled)
    flat = fields.reshape(2 * fields.shape[1], fields.shape[2])
    return jnp.dot(flat, kernel, preferred_element_type=jnp.float32)


def exchange(value, axis, mask):
    count = lax.axis_size(axis)
    return lax.ppermute(value, axis, [(i, i ^ mask) for i in range(count)])


def local(state, prev_slope, positions, pump, detuning, kappa, neighbours, send_list):
    members = state.shape[1]
    rows_here = state.shape[2]
    devices = lax.axis_size(ALL)
    blocks = lax.axis_size("blk")
    group = lax.axis_size("grp")
    scaled = 1.0 / math.sqrt(rows_here * devices)
    section_field = state + section_weight * prev_slope
    section_half = section_field.astype(jnp.bfloat16)
    where_in_group = lax.axis_index("grp")

    me = lax.axis_index(ALL)
    odd = (me % 2) == 1
    listed = jnp.concatenate([send_list[1], send_list[0]])
    pick = (lax.broadcasted_iota(jnp.int32, (rows_here, 1), 0) == listed[None, :]).astype(jnp.float32)
    lists = jnp.dot(
        section_field.reshape(2 * members, rows_here),
        pick,
        precision=lax.Precision.HIGHEST,
        preferred_element_type=jnp.float32,
    ).reshape(2, members, -1)
    halo_width = send_list.shape[1]
    to_prev = lists[:, :, :halo_width]
    to_next = lists[:, :, halo_width:]
    paired = jnp.where(odd, to_prev, to_next)
    crossed = jnp.where(odd, to_next, to_prev)
    crossing = [(i, i + 1) for i in range(1, devices - 1, 2)]
    crossing += [(i, i - 1) for i in range(2, devices, 2)]
    from_crossed = lax.ppermute(crossed, ALL, crossing)

    coded = positions.reshape(2, rows_here // halo_width, halo_width)
    first = exchange(jnp.concatenate([paired, coded], axis=1), "grp", 1)
    from_paired = first[:, :members]
    other = first[:, members:].reshape(2, rows_here)
    targets = jnp.stack([positions, other], axis=1).reshape(2, -1)
    mask = 2
    while mask < group:
        other = exchange(targets, "grp", mask)
        count = targets.shape[1] // rows_here
        targets = jnp.stack(
            [targets.reshape(2, count, rows_here), other.reshape(2, count, rows_here)], axis=2
        ).reshape(2, -1)
        mask *= 2
    width = targets.shape[1]
    from_prev = jnp.where(odd, from_paired, from_crossed)
    from_next = jnp.where(odd, from_crossed, from_paired)

    pieces = jnp.stack(bf16_pieces(positions), axis=1)
    payload = jnp.concatenate([section_half, pieces], axis=1)
    product = block_product(section_half, positions, targets, scaled)
    gathered = payload
    mask = blocks // 2
    while mask >= 1:
        received = exchange(gathered, "blk", mask)
        place = from_pieces(
            received[:, members], received[:, members + 1], received[:, members + 2]
        )
        product = product + block_product(received[:, :members], place, targets, scaled)
        gathered = jnp.concatenate([gathered, received], axis=2)
        mask //= 2
    partial = jnp.stack(
        [
            product[:members, :width] - product[members:, width:],
            product[:members, width:] + product[members:, :width],
        ]
    )

    mask = 1
    while mask < group:
        half = partial.shape[2] // 2
        partial = partial[:, :, :half] + exchange(partial[:, :, half:], "grp", mask)
        mask *= 2
    real_part = partial[0]
    imag_part = partial[1]

    local_buffer = jnp.concatenate([section_field, from_prev, from_next], axis=2)
    places = local_buffer.shape[2]
    hit = neighbours[:, None, :] == lax.broadcasted_iota(jnp.int32, (1, places, 1), 1)
    weights = jnp.sum(jnp.where(hit, kappa[:, None, :], 0.0), axis=0)
    coupled = jnp.dot(
        local_buffer.reshape(2 * members, places),
        weights,
        precision=lax.Precision.HIGHEST,
        preferred_element_type=jnp.float32,
    ).reshape(2, members, rows_here)
    real_field = section_field[0]
    imag_field = section_field[1]
    modulus = real_field * real_field + imag_field * imag_field
    linear_real = pump - modulus
    linear_imag = detuning - alpha_factor * modulus
    local_real = linear_real * real_field - linear_imag * imag_field
    local_imag = linear_real * imag_field + linear_imag * real_field
    slope_real = local_real + real_part - coupled[1]
    slope_imag = local_imag + imag_part + coupled[0]
    return jnp.stack([slope_real, slope_imag])


def solution(mesh):
    placed = (
        P(None, None, ALL),
        P(None, None, ALL),
        P(None, ALL),
        P(ALL),
        P(ALL),
        P(None, ALL),
        P(None, ALL),
        P(None, ALL),
    )
    return jax.shard_map(
        local, mesh=mesh, in_specs=placed, out_specs=P(None, None, ALL), check_vma=False
    )
```

```python
import math

import jax
import jax.numpy as jnp
from jax import lax
from jax.sharding import PartitionSpec as P

section_weight = 0.25
phase_rate = 60.0
alpha_factor = 2.0
ALL = ("blk", "grp")


def bf16_pieces(value):
    high = lax.reduce_precision(value, exponent_bits=8, mantissa_bits=7)
    rest = value - high
    middle = lax.reduce_precision(rest, exponent_bits=8, mantissa_bits=7)
    low = rest - middle
    return [p.astype(jnp.bfloat16) for p in (high, middle, low)]


def from_pieces(high, middle, low):
    f32 = jnp.float32
    return high.astype(f32) + (middle.astype(f32) + low.astype(f32))


def kernel_table(source_place, target_place, scaled):
    horizontal = target_place[0][None, :] - source_place[0][:, None]
    vertical = target_place[1][None, :] - source_place[1][:, None]
    phase = phase_rate * (horizontal * horizontal + vertical * vertical)
    cosine = (scaled * jnp.cos(phase)).astype(jnp.bfloat16)
    sine_part = (scaled * jnp.sin(phase)).astype(jnp.bfloat16)
    return jnp.concatenate([cosine, sine_part], axis=1)


def block_product(fields, source_place, target_place, scaled):
    kernel = kernel_table(source_place, target_place, scaled)
    flat = fields.reshape(2 * fields.shape[1], fields.shape[2])
    return jnp.dot(flat, kernel, preferred_element_type=jnp.float32)


def exchange(value, axis, mask):
    count = lax.axis_size(axis)
    return lax.ppermute(value, axis, [(i, i ^ mask) for i in range(count)])


def local(state, prev_slope, positions, pump, detuning, kappa, neighbours, send_list):
    members = state.shape[1]
    rows_here = state.shape[2]
    devices = lax.axis_size(ALL)
    blocks = lax.axis_size("blk")
    group = lax.axis_size("grp")
    scaled = 1.0 / math.sqrt(rows_here * devices)
    section_field = state + section_weight * prev_slope
    section_half = section_field.astype(jnp.bfloat16)
    where_in_group = lax.axis_index("grp")

    me = lax.axis_index(ALL)
    odd = (me % 2) == 1
    listed = jnp.concatenate([send_list[1], send_list[0]])
    pick = (lax.broadcasted_iota(jnp.int32, (rows_here, 1), 0) == listed[None, :]).astype(jnp.float32)
    lists = jnp.dot(
        section_field.reshape(2 * members, rows_here),
        pick,
        precision=lax.Precision.HIGHEST,
        preferred_element_type=jnp.float32,
    ).reshape(2, members, -1)
    halo_width = send_list.shape[1]
    to_prev = lists[:, :, :halo_width]
    to_next = lists[:, :, halo_width:]
    paired = jnp.where(odd, to_prev, to_next)
    crossed = jnp.where(odd, to_next, to_prev)
    crossing = [(i, i + 1) for i in range(1, devices - 1, 2)]
    crossing += [(i, i - 1) for i in range(2, devices, 2)]
    from_crossed = lax.ppermute(crossed, ALL, crossing)

    coded = positions.reshape(2, rows_here // halo_width, halo_width)
    first = exchange(jnp.concatenate([paired, coded], axis=1), "grp", 1)
    from_paired = first[:, :members]
    other = first[:, members:].reshape(2, rows_here)
    targets = jnp.stack([positions, other], axis=1).reshape(2, -1)
    mask = 2
    while mask < group:
        other = exchange(targets, "grp", mask)
        count = targets.shape[1] // rows_here
        targets = jnp.stack(
            [targets.reshape(2, count, rows_here), other.reshape(2, count, rows_here)], axis=2
        ).reshape(2, -1)
        mask *= 2
    width = targets.shape[1]
    from_prev = jnp.where(odd, from_paired, from_crossed)
    from_next = jnp.where(odd, from_crossed, from_paired)

    pieces = jnp.stack(bf16_pieces(positions), axis=1)
    payload = jnp.concatenate([section_half, pieces], axis=1)
    product = block_product(section_half, positions, targets, scaled)
    def add_blocks(product, received):
        place = from_pieces(
            received[:, members], received[:, members + 1], received[:, members + 2]
        )
        return product + block_product(received[:, :members], place, targets, scaled)

    masks = []
    mask = blocks // 2
    while mask >= 1:
        masks.append(mask)
        mask //= 2
    last = masks[-2:] if len(masks) >= 2 else []
    gathered = payload
    for mask in masks[: len(masks) - len(last)]:
        received = exchange(gathered, "blk", mask)
        product = add_blocks(product, received)
        gathered = jnp.concatenate([gathered, received], axis=2)
    if last:
        for mask in (last[0], last[1], last[0] ^ last[1]):
            product = add_blocks(product, exchange(gathered, "blk", mask))
    partial = jnp.stack(
        [
            product[:members, :width] - product[members:, width:],
            product[:members, width:] + product[members:, :width],
        ]
    )

    mask = 1
    while mask < group:
        half = partial.shape[2] // 2
        partial = partial[:, :, :half] + exchange(partial[:, :, half:], "grp", mask)
        mask *= 2
    real_part = partial[0]
    imag_part = partial[1]

    local_buffer = jnp.concatenate([section_field, from_prev, from_next], axis=2)
    places = local_buffer.shape[2]
    hit = neighbours[:, None, :] == lax.broadcasted_iota(jnp.int32, (1, places, 1), 1)
    weights = jnp.sum(jnp.where(hit, kappa[:, None, :], 0.0), axis=0)
    coupled = jnp.dot(
        local_buffer.reshape(2 * members, places),
        weights,
        precision=lax.Precision.HIGHEST,
        preferred_element_type=jnp.float32,
    ).reshape(2, members, rows_here)
    real_field = section_field[0]
    imag_field = section_field[1]
    modulus = real_field * real_field + imag_field * imag_field
    linear_real = pump - modulus
    linear_imag = detuning - alpha_factor * modulus
    local_real = linear_real * real_field - linear_imag * imag_field
    local_imag = linear_real * imag_field + linear_imag * real_field
    slope_real = local_real + real_part - coupled[1]
    slope_imag = local_imag + imag_part + coupled[0]
    return jnp.stack([slope_real, slope_imag])


def solution(mesh):
    placed = (
        P(None, None, ALL),
        P(None, None, ALL),
        P(None, ALL),
        P(ALL),
        P(ALL),
        P(None, ALL),
        P(None, ALL),
        P(None, ALL),
    )
    return jax.shard_map(
        local, mesh=mesh, in_specs=placed, out_specs=P(None, None, ALL), check_vma=False
    )
```
